512 devices in a mesh: row: 64 (over z_lo, x, core), col: 8 (over y, z_hi).
Axes of the slice: x: 4, y: 4, z: 16 (z_hi: 2, z_lo: 8; z = z_hi * 8 + z_lo), core: 2. Of those that a mesh axis runs over, the one named last changes fastest.
Arguments:
- u3: bfloat16 [2048, 64, 512], P(('row', 'col')), may hold values from -6 to 6
- g3: bfloat16 [2048, 64, 512], P(('row', 'col')), may hold values from -6 to 6
- ln3_w: float32 [512], replicated, may hold values from 0.25 to 1.75
- ln3_b: float32 [512], replicated, may hold values from -3 to 3
- bias3: float32 [2048], replicated, may hold values from -3 to 3
- gamma3: float32 [512], replicated, may hold values from 0.3 to 1.5
- kernel3: float32 [7, 7, 512], replicated, may hold values from -0.875 to 0.875
- expand3: bfloat16 [512, 2048], P(None, 'row'), may hold values from -0.25 to 0.25
- project3: bfloat16 [512, 2048], P(None, 'row'), may hold values from -0.125 to 0.125
- down_w: bfloat16 [1024, 512], P(None, 'row'), may hold values from -0.1875 to 0.1875
- dln_w: float32 [256], replicated, may hold values from 0.25 to 1.75
- y2: bfloat16 [4096, 128, 256], P('row', 'col'), may hold values from -6 to 6
- u2: bfloat16 [4096, 128, 256], P('row', 'col'), may hold values from -6 to 6
- ln2_w: float32 [256], replicated, may hold values from 0.25 to 1.75
- ln2_b: float32 [256], replicated, may hold values from -3 to 3
- bias2: float32 [1024], replicated, may hold values from -3 to 3
- gamma2: float32 [256], replicated, may hold values from 0.3 to 1.5
- kernel2: float32 [7, 7, 256], replicated, may hold values from -0.875 to 0.875
- expand2: bfloat16 [256, 1024], P(None, 'row'), may hold values from -0.375 to 0.375
- project2: bfloat16 [256, 1024], P(None, 'row'), may hold values from -0.1875 to 0.1875
- tissue: int32 [256, 8], P('row', 'col'), may hold values 0 or 1
Outputs:
- gx2: bfloat16 [4096, 128, 256], P('row', 'col')
The draws below stay inside these ranges and needn't reach their ends.
Inputs may be any that keep to these rules, and one draw needn't show every extreme that they name: tissue marks tiles holding tissue.
All inputs are finite; a program needn't handle non-finite values. No bound on the sum of `tissue` on one device may be relied on, other than what follows from the above.
Results may differ from the reference program's by a relative error of at most 0.014.
Values may be sent and summed in bfloat16 or wider, within the bound.
No kernel may reach another device: no remote copies, remote signals or barrier semaphores. Data moves between devices by JAX's collectives and lax.ppermute only.
A program may use at most 64 MiB of HBM per device.

```python
import math
import jax
import jax.numpy as jnp
from jax import lax

C2 = 256
C3 = 512
HID2 = 1024
HID3 = 2048
KSIZE = 7
TILE = 16
H2 = 4096
W2 = 128
H3 = 2048
W3 = 64


def place_ends(values, key, least, high):
    dims = values.shape
    spot = [jax.random.randint(jax.random.fold_in(key, axis), (), 0, dims[axis]) for axis in range(len(dims))]
    values = values.at[tuple(spot)].set(least)
    longest = dims.index(max(dims))
    spot[longest] = (spot[longest] + 1) % dims[longest]
    return values.at[tuple(spot)].set(high)


def block_levels(own_key, dims, split, least, largest):
    def one(dim, parts):
        heights = jax.random.uniform(jax.random.fold_in(jax.random.fold_in(own_key, 6), dim), (parts,), jnp.float32, least / len(split), largest / len(split))
        return jnp.repeat(jnp.exp(heights), dims[dim] // parts).reshape((-1,) + (1,) * (len(dims) - dim - 1))

    level = one(*split[0])
    for cut in split[1:]:
        level = level * one(*cut)
    return level


def noise(rng, shape, scale, reach, split=(), held_as=jnp.bfloat16):
    drawn = jax.random.normal(rng, shape, jnp.float32) * scale
    if len(split) > 0:
        drawn = block_levels(rng, shape, split, -0.22, 0.18) * drawn
    return jnp.clip(drawn, min=-reach, max=reach).astype(held_as)


def setup_inputs(seed: int = 0) -> dict:
    keys = jax.random.split(jax.random.key(seed), 22)
    return {
        "u3": noise(keys[0], (H3, W3, C3), 1.0, 6.0, ((0, 512),)),
        "g3": noise(keys[1], (H3, W3, C3), 1.0, 6.0, ((0, 512),)),
        "ln3_w": jnp.clip(1.0 + 0.15 * jax.random.normal(keys[2], (C3,), jnp.float32), 0.25, 1.75),
        "ln3_b": noise(keys[3], (C3,), 0.5, 3.0, (), jnp.float32),
        "bias3": noise(keys[4], (HID3,), 0.5, 3.0, (), jnp.float32),
        "gamma3": jnp.clip(jnp.exp(jax.random.uniform(keys[5], (C3,), jnp.float32, math.log(0.3), math.log(1.5))), 0.3, 1.5),
        "kernel3": noise(keys[6], (KSIZE, KSIZE, C3), (KSIZE * KSIZE) ** -0.5, 0.875, (), jnp.float32),
        "expand3": noise(keys[7], (C3, HID3), C3 ** -0.5, 0.25, ((1, 64),)),
        "project3": noise(keys[8], (C3, HID3), HID3 ** -0.5, 0.125, ((1, 64),)),
        "down_w": noise(keys[9], (4 * C2, C3), (4 * C2) ** -0.5, 0.1875, ((1, 64),)),
        "dln_w": jnp.clip(1.0 + 0.15 * jax.random.normal(keys[10], (C2,), jnp.float32), 0.25, 1.75),
        "y2": noise(keys[11], (H2, W2, C2), 1.0, 6.0, ((0, 64), (1, 8))),
        "u2": noise(keys[12], (H2, W2, C2), 1.0, 6.0, ((0, 64), (1, 8))),
        "ln2_w": jnp.clip(1.0 + 0.15 * jax.random.normal(keys[13], (C2,), jnp.float32), 0.25, 1.75),
        "ln2_b": noise(keys[14], (C2,), 0.5, 3.0, (), jnp.float32),
        "bias2": noise(keys[15], (HID2,), 0.5, 3.0, (), jnp.float32),
        "gamma2": jnp.clip(jnp.exp(jax.random.uniform(keys[16], (C2,), jnp.float32, math.log(0.3), math.log(1.5))), 0.3, 1.5),
        "kernel2": noise(keys[17], (KSIZE, KSIZE, C2), (KSIZE * KSIZE) ** -0.5, 0.875, (), jnp.float32),
        "expand2": noise(keys[18], (C2, HID2), C2 ** -0.5, 0.375, ((1, 64),)),
        "project2": noise(keys[19], (C2, HID2), HID2 ** -0.5, 0.1875, ((1, 64),)),
        "tissue": place_ends((jax.random.randint(keys[20], (H2 // TILE, W2 // TILE), 0, 4) < 3).astype(jnp.int32), jax.random.fold_in(keys[20], 1), 0, 1),
    }


EPS = 1e-06
ROOT_HALF = 0.7071067811865476
DENS = 0.3989422804014327

def block_grad(u, g, layernorm_weight, layernorm_bias, bias, gamma, expand, project):
    count = u.shape[0]
    width = u.shape[1]
    blk = min(count, 512)

    def one(pair):
        ub, gb = pair
        uf = ub.astype(jnp.float32)
        centered_input = uf - lax.optimization_barrier(jnp.mean(uf, axis=-1, keepdims=True))
        inverse_deviation = lax.rsqrt(lax.optimization_barrier(jnp.mean(centered_input * centered_input, axis=-1, keepdims=True)) + EPS)
        standardized_input = centered_input * inverse_deviation
        normalized_output = (standardized_input * layernorm_weight + layernorm_bias).astype(jnp.bfloat16)
        hidden = jnp.dot(normalized_output, expand, preferred_element_type=jnp.float32) + bias
        scaled = (gamma * gb.astype(jnp.float32)).astype(jnp.bfloat16)
        grad_act = jnp.dot(scaled, project, preferred_element_type=jnp.float32)
        slope = 0.5 * (1.0 + jax.scipy.special.erf(hidden * ROOT_HALF)) + hidden * DENS * jnp.exp(-0.5 * hidden * hidden)
        grad_hid = (grad_act * slope).astype(jnp.bfloat16)
        grad_norm = lax.dot_general(grad_hid, expand, (((1,), (1,)), ((), ())), preferred_element_type=jnp.float32)
        projection_term = grad_norm * layernorm_weight
        upstream_gradient = inverse_deviation * (projection_term - lax.optimization_barrier(jnp.mean(projection_term, axis=-1, keepdims=True)) - standardized_input * lax.optimization_barrier(jnp.mean(projection_term * standardized_input, axis=-1, keepdims=True)))
        return upstream_gradient.astype(jnp.bfloat16)
    result = lax.map(one, (u.reshape(count // blk, blk, width), g.reshape(count // blk, blk, width)))
    return result.reshape(count, width)

def spread(padded, kernel, height, width):
    total = jnp.zeros((height, width, padded.shape[2]), jnp.float32)
    for dy in range(7):
        for dx in range(7):
            total = total + kernel[dy, dx] * padded[6 - dy:6 - dy + height, 6 - dx:6 - dx + width].astype(jnp.float32)
    return total

def norm_back(value, grad, gain):
    vf = value.astype(jnp.float32)
    centered_input = vf - lax.optimization_barrier(jnp.mean(vf, axis=-1, keepdims=True))
    inverse_deviation = lax.rsqrt(lax.optimization_barrier(jnp.mean(centered_input * centered_input, axis=-1, keepdims=True)) + EPS)
    yhat = centered_input * inverse_deviation
    projection_term = grad * gain
    return inverse_deviation * (projection_term - lax.optimization_barrier(jnp.mean(projection_term, axis=-1, keepdims=True)) - yhat * lax.optimization_barrier(jnp.mean(projection_term * yhat, axis=-1, keepdims=True)))

def reference(u3, g3, ln3_w, ln3_b, bias3, gamma3, kernel3, expand3, project3, down_w, dln_w, y2, u2, ln2_w, ln2_b, bias2, gamma2, kernel2, expand2, project2, tissue):
    height3, width3, chans3 = u3.shape
    grad_u3 = block_grad(u3.reshape(-1, chans3), g3.reshape(-1, chans3), ln3_w, ln3_b, bias3, gamma3, expand3, project3).reshape(u3.shape)
    padded3 = jnp.pad(grad_u3, ((3, 3), (3, 3), (0, 0)))
    gx3 = (g3.astype(jnp.float32) + spread(padded3, kernel3, height3, width3)).astype(jnp.bfloat16)
    chans2 = y2.shape[2]
    grad_m = lax.dot_general(gx3.reshape(-1, chans3), down_w, (((1,), (1,)), ((), ())), preferred_element_type=jnp.float32)
    grad_m = lax.optimization_barrier(grad_m.astype(jnp.bfloat16)).astype(jnp.float32)
    grad_m = grad_m.reshape(height3, width3, 2, 2, chans2).transpose(0, 2, 1, 3, 4).reshape(2 * height3, 2 * width3, chans2)
    grad_y = norm_back(y2, grad_m, dln_w)
    pixel_mask = jnp.repeat(jnp.repeat(tissue, TILE, axis=0), TILE, axis=1).astype(jnp.float32)
    g2 = (grad_y * pixel_mask[:, :, None]).astype(jnp.bfloat16)
    height2, width2 = (y2.shape[0], y2.shape[1])
    grad_u2 = block_grad(u2.reshape(-1, chans2), g2.reshape(-1, chans2), ln2_w, ln2_b, bias2, gamma2, expand2, project2).reshape(u2.shape)
    padded2 = jnp.pad(grad_u2, ((3, 3), (3, 3), (0, 0)))
    return (g2.astype(jnp.float32) + spread(padded2, kernel2, height2, width2)).astype(jnp.bfloat16)
```

```python
import jax
import jax.numpy as jnp
from jax import lax
from jax.sharding import Mesh
from jax.sharding import PartitionSpec as P


ROW = ("zl", "x", "core")
COL = ("y", "zh")
STAGES = (("zl", 8), ("x", 4), ("core", 2))

TILE = 16


EPS = 1e-06
ROOT_HALF = 0.7071067811865476
DENS = 0.3989422804014327


def padded_2(block, sides, width):
    for axis, dim in sides:
        count = lax.axis_size(axis)
        forward = [(i, i + 1) for i in range(count - 1)]
        backward = [(target, source) for source, target in forward]
        low = lax.ppermute(
            lax.slice_in_dim(block, block.shape[dim] - width, None, axis=dim), axis, forward
        )
        high = lax.ppermute(lax.slice_in_dim(block, 0, width, axis=dim), axis, backward)
        block = jnp.concatenate([low, block, high], axis=dim)
    return block


def shifted_gather(block, axis, count):
    parts = [block]
    for shift in range(1, count):
        pairs = [(i, (i + shift) % count) for i in range(count)]
        parts.append(lax.ppermute(block, axis, pairs))
    return jnp.concatenate(parts, axis=0)


def gather_weights(pieces):
    flat = jnp.concatenate([p.reshape(-1, 128) for p in pieces], axis=0)
    for axis, count in STAGES:
        flat = shifted_gather(flat, axis, count)
    slabs = flat.reshape(64, -1, 128)
    r = jnp.arange(64)
    s_core, s_x, s_zl = r // 32, (r // 8) % 4, r % 8
    zl = (lax.axis_index("zl") - s_zl) % 8
    xx = (lax.axis_index("x") - s_x) % 4
    cc = (lax.axis_index("core") - s_core) % 2
    source = (zl * 4 + xx) * 2 + cc
    return slabs, source


def block_grad(u, g, layernorm_weight, layernorm_bias, bias, gamma, expand, project):
    count = u.shape[0]
    width = u.shape[1]
    blk = min(count, 512)

    def one(pair):
        ub, gb = pair
        uf = ub.astype(jnp.float32)
        centered_input = uf - jnp.mean(uf, axis=-1, keepdims=True)
        inverse_deviation = lax.rsqrt(
            jnp.mean(centered_input * centered_input, axis=-1, keepdims=True) + EPS
        )
        standardized_input = centered_input * inverse_deviation
        normalized_output = (standardized_input * layernorm_weight + layernorm_bias).astype(
            jnp.bfloat16
        )
        hidden = jnp.dot(normalized_output, expand, preferred_element_type=jnp.float32) + bias
        scaled = (gamma * gb.astype(jnp.float32)).astype(jnp.bfloat16)
        grad_act = jnp.dot(scaled, project, preferred_element_type=jnp.float32)
        slope = 0.5 * (1.0 + jax.scipy.special.erf(hidden * ROOT_HALF)) + hidden * DENS * jnp.exp(
            -0.5 * hidden * hidden
        )
        grad_hid = (grad_act * slope).astype(jnp.bfloat16)
        grad_norm = lax.dot_general(
            grad_hid, expand, (((1,), (1,)), ((), ())), preferred_element_type=jnp.float32
        )
        projection_term = grad_norm * layernorm_weight
        upstream_gradient = inverse_deviation * (
            projection_term
            - jnp.mean(projection_term, axis=-1, keepdims=True)
            - standardized_input
            * jnp.mean(projection_term * standardized_input, axis=-1, keepdims=True)
        )
        return upstream_gradient.astype(jnp.bfloat16)

    result = lax.map(
        one, (u.reshape(count // blk, blk, width), g.reshape(count // blk, blk, width))
    )
    return result.reshape(count, width)


def spread(padded, kernel, height, width):
    total = jnp.zeros((height, width, padded.shape[2]), jnp.float32)
    for dy in range(7):
        for dx in range(7):
            total = total + kernel[dy, dx] * padded[
                6 - dy : 6 - dy + height, 6 - dx : 6 - dx + width
            ].astype(jnp.float32)
    return total


def norm_back(value, grad, gain):
    vf = value.astype(jnp.float32)
    centered_input = vf - jnp.mean(vf, axis=-1, keepdims=True)
    inverse_deviation = lax.rsqrt(
        jnp.mean(centered_input * centered_input, axis=-1, keepdims=True) + EPS
    )
    yhat = centered_input * inverse_deviation
    projection_term = grad * gain
    return inverse_deviation * (
        projection_term
        - jnp.mean(projection_term, axis=-1, keepdims=True)
        - yhat * jnp.mean(projection_term * yhat, axis=-1, keepdims=True)
    )


def project_down(grads, down_whole):
    return lax.dot_general(
        grads, down_whole, (((1,), (1,)), ((), ())), preferred_element_type=jnp.float32
    )


def on_device(
    u3,
    g3,
    ln3_w,
    ln3_b,
    bias3,
    gamma3,
    kernel3,
    expand3,
    project3,
    down_w,
    dln_w,
    y2,
    u2,
    ln2_w,
    ln2_b,
    bias2,
    gamma2,
    kernel2,
    expand2,
    project2,
    tissue,
):
    slabs, source = gather_weights((expand3, project3, down_w, expand2, project2))
    n3 = expand3.size // 128
    n2 = expand2.size // 128
    nd = down_w.size // 128
    cut = (0, n3, 2 * n3, 2 * n3 + nd, 2 * n3 + nd + n2, 2 * n3 + nd + 2 * n2)

    def widen(i, shard_shape):
        part = slabs[:, cut[i] : cut[i + 1]].reshape((64,) + shard_shape)
        return part.transpose(1, 0, 2).reshape(shard_shape[0], 64 * shard_shape[1])

    expand3 = widen(0, expand3.shape)
    project3 = widen(1, project3.shape)
    expand2 = widen(3, expand2.shape)
    project2 = widen(4, project2.shape)
    bias3 = bias3.reshape(64, -1)[source].reshape(-1)
    bias2 = bias2.reshape(64, -1)[source].reshape(-1)
    r = jnp.arange(64)
    zl_a, x_a, c_a = r // 8, (r // 2) % 4, r % 2
    slot = (
        ((lax.axis_index("core") - c_a) % 2) * 32
        + ((lax.axis_index("x") - x_a) % 4) * 8
        + (lax.axis_index("zl") - zl_a) % 8
    )
    down_parts = slabs[:, cut[2] : cut[3]].reshape((64,) + down_w.shape)[slot]
    down_w = down_parts.transpose(1, 0, 2).reshape(down_w.shape[0], 64 * down_w.shape[1])
    rows3, width3, chans3 = u3.shape
    rows2, cols2, chans2 = y2.shape
    grad_u3 = block_grad(
        u3.reshape(-1, chans3),
        g3.reshape(-1, chans3),
        ln3_w,
        ln3_b,
        bias3,
        gamma3,
        expand3,
        project3,
    ).reshape(u3.shape)
    rimmed3 = padded_2(grad_u3, ((ROW + COL, 0),), 3)
    padded3 = jnp.pad(rimmed3, ((0, 0), (3, 3), (0, 0)))
    gx3 = (g3.astype(jnp.float32) + spread(padded3, kernel3, rows3, width3)).astype(jnp.bfloat16)
    grad_m = project_down(gx3.reshape(-1, chans3), down_w).astype(jnp.bfloat16)
    grad_m = grad_m.reshape(rows3, width3, 4 * chans2)
    moved = lax.all_to_all(grad_m, COL, split_axis=1, concat_axis=0, tiled=True)
    grad_mf = moved.astype(jnp.float32)
    grad_mf = (
        grad_mf.reshape(rows2 // 2, cols2 // 2, 2, 2, chans2)
        .transpose(0, 2, 1, 3, 4)
        .reshape(rows2, cols2, chans2)
    )
    grad_y = norm_back(y2, grad_mf, dln_w)
    tile_rows, tile_cols = tissue.shape
    pixel_mask = jnp.broadcast_to(
        tissue.astype(jnp.float32)[:, None, :, None], (tile_rows, TILE, tile_cols, TILE)
    ).reshape(rows2, cols2)
    g2 = (grad_y * pixel_mask[:, :, None]).astype(jnp.bfloat16)
    grad_u2 = block_grad(
        u2.reshape(-1, chans2),
        g2.reshape(-1, chans2),
        ln2_w,
        ln2_b,
        bias2,
        gamma2,
        expand2,
        project2,
    ).reshape(u2.shape)
    padded2 = padded_2(grad_u2, ((ROW, 0), (COL, 1)), 3)
    return (g2.astype(jnp.float32) + spread(padded2, kernel2, rows2, cols2)).astype(jnp.bfloat16)


def solution(mesh):
    sizes = tuple(n for _, n in STAGES) + (4, 2)
    mesh = Mesh(mesh.devices.reshape(sizes), ROW + COL)
    placed = (
        P(ROW + COL, None, None),
        P(ROW + COL, None, None),
        P(),
        P(),
        P(),
        P(),
        P(),
        P(None, ROW),
        P(None, ROW),
        P(None, ROW),
        P(),
        P(ROW, COL, None),
        P(ROW, COL, None),
        P(),
        P(),
        P(),
        P(),
        P(),
        P(None, ROW),
        P(None, ROW),
        P(ROW, COL),
    )
    return jax.shard_map(
        on_device, mesh=mesh, in_specs=placed, out_specs=P(ROW, COL, None), check_vma=False
    )
```

```python
import jax
import jax.numpy as jnp
from jax import lax
from jax.sharding import Mesh
from jax.sharding import PartitionSpec as P


ROW = ("zl", "x", "core")
COL = ("y", "zh")
STAGES = (("zl", 8), ("x", 4), ("core", 2))

TILE = 16


EPS = 1e-06
ROOT_HALF = 0.7071067811865476
DENS = 0.3989422804014327


def padded_2(block, sides, width):
    for axis, dim in sides:
        count = lax.axis_size(axis)
        forward = [(i, i + 1) for i in range(count - 1)]
        backward = [(target, source) for source, target in forward]
        low = lax.ppermute(
            lax.slice_in_dim(block, block.shape[dim] - width, None, axis=dim), axis, forward
        )
        high = lax.ppermute(lax.slice_in_dim(block, 0, width, axis=dim), axis, backward)
        block = jnp.concatenate([low, block, high], axis=dim)
    return block


def shifted_gather(block, axis, count):
    parts = [block]
    for shift in range(1, count):
        pairs = [(i, (i + shift) % count) for i in range(count)]
        parts.append(lax.ppermute(block, axis, pairs))
    return jnp.concatenate(parts, axis=0)


def gather_weights(pieces):
    flat = jnp.concatenate([p.reshape(-1, 512) for p in pieces], axis=0)
    for axis, count in STAGES:
        flat = shifted_gather(flat, axis, count)
    slabs = flat.reshape(64, -1, 512)
    r = jnp.arange(64)
    s_core, s_x, s_zl = r // 32, (r // 8) % 4, r % 8
    zl = (lax.axis_index("zl") - s_zl) % 8
    xx = (lax.axis_index("x") - s_x) % 4
    cc = (lax.axis_index("core") - s_core) % 2
    source = (zl * 4 + xx) * 2 + cc
    return slabs, source


def block_grad(u, g, layernorm_weight, layernorm_bias, bias, gamma, expand_t, project_t):
    def one(pair):
        ub, gb = pair
        uf = ub.astype(jnp.float32)
        centered_input = uf - jnp.mean(uf, axis=-1, keepdims=True)
        inverse_deviation = lax.rsqrt(
            jnp.mean(centered_input * centered_input, axis=-1, keepdims=True) + EPS
        )
        standardized_input = centered_input * inverse_deviation
        normalized_output = (standardized_input * layernorm_weight + layernorm_bias).astype(
            jnp.bfloat16
        )
        hidden = (
            lax.dot_general(
                normalized_output, expand_t, (((1,), (1,)), ((), ())),
                preferred_element_type=jnp.float32,
            )
            + bias
        )
        scaled = (gamma * gb.astype(jnp.float32)).astype(jnp.bfloat16)
        grad_act = lax.dot_general(
            scaled, project_t, (((1,), (1,)), ((), ())), preferred_element_type=jnp.float32
        )
        slope = 0.5 * (1.0 + jax.scipy.special.erf(hidden * ROOT_HALF)) + hidden * DENS * jnp.exp(
            -0.5 * hidden * hidden
        )
        grad_hid = (grad_act * slope).astype(jnp.bfloat16)
        grad_norm = jnp.dot(grad_hid, expand_t, preferred_element_type=jnp.float32)
        projection_term = grad_norm * layernorm_weight
        upstream_gradient = inverse_deviation * (
            projection_term
            - jnp.mean(projection_term, axis=-1, keepdims=True)
            - standardized_input
            * jnp.mean(projection_term * standardized_input, axis=-1, keepdims=True)
        )
        return upstream_gradient.astype(jnp.bfloat16)

    return one((u, g))


def spread(padded, kernel, height, width):
    total = jnp.zeros((height, width, padded.shape[2]), jnp.float32)
    for dy in range(7):
        for dx in range(7):
            total = total + kernel[dy, dx] * padded[
                6 - dy : 6 - dy + height, 6 - dx : 6 - dx + width
            ].astype(jnp.float32)
    return total


def norm_back(value, grad, gain):
    vf = value.astype(jnp.float32)
    centered_input = vf - jnp.mean(vf, axis=-1, keepdims=True)
    inverse_deviation = lax.rsqrt(
        jnp.mean(centered_input * centered_input, axis=-1, keepdims=True) + EPS
    )
    yhat = centered_input * inverse_deviation
    projection_term = grad * gain
    return inverse_deviation * (
        projection_term
        - jnp.mean(projection_term, axis=-1, keepdims=True)
        - yhat * jnp.mean(projection_term * yhat, axis=-1, keepdims=True)
    )


def project_down(grads, down_t):
    return jnp.dot(grads, down_t, preferred_element_type=jnp.float32)


def on_device(
    u3,
    g3,
    ln3_w,
    ln3_b,
    bias3,
    gamma3,
    kernel3,
    expand3,
    project3,
    down_w,
    dln_w,
    y2,
    u2,
    ln2_w,
    ln2_b,
    bias2,
    gamma2,
    kernel2,
    expand2,
    project2,
    tissue,
):
    pieces = (expand3.T, project3.T, down_w.T, expand2.T, project2.T)
    slabs, source = gather_weights(pieces)
    cut = [0]
    for p in pieces:
        cut.append(cut[-1] + p.size // 512)

    def stacked(i):
        part = slabs[:, cut[i] : cut[i + 1]].reshape((64,) + pieces[i].shape)
        return part.reshape(64 * pieces[i].shape[0], pieces[i].shape[1])

    expand3 = stacked(0)
    project3 = stacked(1)
    expand2 = stacked(3)
    project2 = stacked(4)
    bias3 = bias3.reshape(64, -1)[source].reshape(-1)
    bias2 = bias2.reshape(64, -1)[source].reshape(-1)
    r = jnp.arange(64)
    zl_a, x_a, c_a = r // 8, (r // 2) % 4, r % 2
    slot = (
        ((lax.axis_index("core") - c_a) % 2) * 32
        + ((lax.axis_index("x") - x_a) % 4) * 8
        + (lax.axis_index("zl") - zl_a) % 8
    )
    down_parts = slabs[:, cut[2] : cut[3]].reshape((64,) + pieces[2].shape)[slot]
    down_t = down_parts.reshape(64 * pieces[2].shape[0], pieces[2].shape[1])
    rows3, width3, chans3 = u3.shape
    rows2, cols2, chans2 = y2.shape
    grad_u3 = block_grad(
        u3.reshape(-1, chans3),
        g3.reshape(-1, chans3),
        ln3_w,
        ln3_b,
        bias3,
        gamma3,
        expand3,
        project3,
    ).reshape(u3.shape)
    rimmed3 = padded_2(grad_u3, ((ROW + COL, 0),), 3)
    padded3 = jnp.pad(rimmed3, ((0, 0), (3, 3), (0, 0)))
    gx3 = (g3.astype(jnp.float32) + spread(padded3, kernel3, rows3, width3)).astype(jnp.bfloat16)
    moved = lax.all_to_all(gx3, COL, split_axis=1, concat_axis=0, tiled=True)
    grad_m = project_down(moved.reshape(-1, chans3), down_t).astype(jnp.bfloat16)
    grad_mf = grad_m.astype(jnp.float32)
    grad_mf = (
        grad_mf.reshape(rows2 // 2, cols2 // 2, 2, 2, chans2)
        .transpose(0, 2, 1, 3, 4)
        .reshape(rows2, cols2, chans2)
    )
    grad_y = norm_back(y2, grad_mf, dln_w)
    tile_rows, tile_cols = tissue.shape
    pixel_mask = jnp.broadcast_to(
        tissue.astype(jnp.float32)[:, None, :, None], (tile_rows, TILE, tile_cols, TILE)
    ).reshape(rows2, cols2)
    g2 = (grad_y * pixel_mask[:, :, None]).astype(jnp.bfloat16)
    grad_u2 = block_grad(
        u2.reshape(-1, chans2),
        g2.reshape(-1, chans2),
        ln2_w,
        ln2_b,
        bias2,
        gamma2,
        expand2,
        project2,
    ).reshape(u2.shape)
    padded2 = padded_2(grad_u2, ((ROW, 0), (COL, 1)), 3)
    return (g2.astype(jnp.float32) + spread(padded2, kernel2, rows2, cols2)).astype(jnp.bfloat16)


def solution(mesh):
    sizes = tuple(n for _, n in STAGES) + (4, 2)
    mesh = Mesh(mesh.devices.reshape(sizes), ROW + COL)
    placed = (
        P(ROW + COL, None, None),
        P(ROW + COL, None, None),
        P(),
        P(),
        P(),
        P(),
        P(),
        P(None, ROW),
        P(None, ROW),
        P(None, ROW),
        P(),
        P(ROW, COL, None),
        P(ROW, COL, None),
        P(),
        P(),
        P(),
        P(),
        P(),
        P(None, ROW),
        P(None, ROW),
        P(ROW, COL),
    )
    return jax.shard_map(
        on_device, mesh=mesh, in_specs=placed, out_specs=P(ROW, COL, None), check_vma=False
    )
```

```python
import jax
import jax.numpy as jnp
from jax import lax
from jax.sharding import Mesh
from jax.sharding import PartitionSpec as P


ROW = ("zl", "x", "core")
COL = ("y", "zh")
STAGES = (("zl", 8), ("x", 4), ("core", 2))

TILE = 16


EPS = 1e-06
ROOT_HALF = 0.7071067811865476
DENS = 0.3989422804014327


def padded_2(block, sides, width):
    for axis, dim in sides:
        count = lax.axis_size(axis)
        forward = [(i, i + 1) for i in range(count - 1)]
        backward = [(target, source) for source, target in forward]
        low = lax.ppermute(
            lax.slice_in_dim(block, block.shape[dim] - width, None, axis=dim), axis, forward
        )
        high = lax.ppermute(lax.slice_in_dim(block, 0, width, axis=dim), axis, backward)
        block = jnp.concatenate([low, block, high], axis=dim)
    return block


def shifted_gather(block, axis, count):
    parts = [block]
    for shift in range(1, count):
        pairs = [(i, (i + shift) % count) for i in range(count)]
        parts.append(lax.ppermute(block, axis, pairs))
    return jnp.concatenate(parts, axis=0)


def ring_gather(block):
    def lin(z):
        return (z % 8) * 2 + z // 8

    parts = [block]
    for shift in range(1, 8):
        step = shift if shift <= 4 else shift - 8
        pairs = [(lin(z), lin((z + step) % 16)) for z in range(16)]
        parts.append(lax.ppermute(block, ("zl", "zh"), pairs))
    return jnp.concatenate(parts, axis=0)


def gather_weights(pieces):
    flat = jnp.concatenate([p.reshape(-1, 512) for p in pieces], axis=0)
    flat = ring_gather(flat)
    for axis, count in STAGES[1:]:
        flat = shifted_gather(flat, axis, count)
    slabs = flat.reshape(64, -1, 512)
    r = jnp.arange(64)
    s_core, s_x, s_zl = r // 32, (r // 8) % 4, r % 8
    zl = (lax.axis_index("zl") - s_zl) % 8
    xx = (lax.axis_index("x") - s_x) % 4
    cc = (lax.axis_index("core") - s_core) % 2
    source = (zl * 4 + xx) * 2 + cc
    return slabs, source


def block_grad(u, g, layernorm_weight, layernorm_bias, bias, gamma, expand_t, project_t):
    def one(pair):
        ub, gb = pair
        uf = ub.astype(jnp.float32)
        centered_input = uf - jnp.mean(uf, axis=-1, keepdims=True)
        inverse_deviation = lax.rsqrt(
            jnp.mean(centered_input * centered_input, axis=-1, keepdims=True) + EPS
        )
        standardized_input = centered_input * inverse_deviation
        normalized_output = (standardized_input * layernorm_weight + layernorm_bias).astype(
            jnp.bfloat16
        )
        hidden = (
            lax.dot_general(
                normalized_output, expand_t, (((1,), (1,)), ((), ())),
                preferred_element_type=jnp.float32,
            )
            + bias
        )
        scaled = (gamma * gb.astype(jnp.float32)).astype(jnp.bfloat16)
        grad_act = lax.dot_general(
            scaled, project_t, (((1,), (1,)), ((), ())), preferred_element_type=jnp.float32
        )
        slope = 0.5 * (1.0 + jax.scipy.special.erf(hidden * ROOT_HALF)) + hidden * DENS * jnp.exp(
            -0.5 * hidden * hidden
        )
        grad_hid = (grad_act * slope).astype(jnp.bfloat16)
        grad_norm = jnp.dot(grad_hid, expand_t, preferred_element_type=jnp.float32)
        projection_term = grad_norm * layernorm_weight
        upstream_gradient = inverse_deviation * (
            projection_term
            - jnp.mean(projection_term, axis=-1, keepdims=True)
            - standardized_input
            * jnp.mean(projection_term * standardized_input, axis=-1, keepdims=True)
        )
        return upstream_gradient.astype(jnp.bfloat16)

    return one((u, g))


def spread(padded, kernel, height, width):
    total = jnp.zeros((height, width, padded.shape[2]), jnp.float32)
    for dy in range(7):
        for dx in range(7):
            total = total + kernel[dy, dx] * padded[
                6 - dy : 6 - dy + height, 6 - dx : 6 - dx + width
            ].astype(jnp.float32)
    return total


def norm_back(value, grad, gain):
    vf = value.astype(jnp.float32)
    centered_input = vf - jnp.mean(vf, axis=-1, keepdims=True)
    inverse_deviation = lax.rsqrt(
        jnp.mean(centered_input * centered_input, axis=-1, keepdims=True) + EPS
    )
    yhat = centered_input * inverse_deviation
    projection_term = grad * gain
    return inverse_deviation * (
        projection_term
        - jnp.mean(projection_term, axis=-1, keepdims=True)
        - yhat * jnp.mean(projection_term * yhat, axis=-1, keepdims=True)
    )


def project_down(grads, down_t):
    return jnp.dot(grads, down_t, preferred_element_type=jnp.float32)


def on_device(
    u3,
    g3,
    ln3_w,
    ln3_b,
    bias3,
    gamma3,
    kernel3,
    expand3,
    project3,
    down_w,
    dln_w,
    y2,
    u2,
    ln2_w,
    ln2_b,
    bias2,
    gamma2,
    kernel2,
    expand2,
    project2,
    tissue,
):
    pieces = (expand3.T, project3.T, down_w.T, expand2.T, project2.T)
    slabs, source = gather_weights(pieces)
    cut = [0]
    for p in pieces:
        cut.append(cut[-1] + p.size // 512)

    def stacked(i):
        part = slabs[:, cut[i] : cut[i + 1]].reshape((64,) + pieces[i].shape)
        return part.reshape(64 * pieces[i].shape[0], pieces[i].shape[1])

    expand3 = stacked(0)
    project3 = stacked(1)
    expand2 = stacked(3)
    project2 = stacked(4)
    bias3 = bias3.reshape(64, -1)[source].reshape(-1)
    bias2 = bias2.reshape(64, -1)[source].reshape(-1)
    r = jnp.arange(64)
    zl_a, x_a, c_a = r // 8, (r // 2) % 4, r % 2
    slot = (
        ((lax.axis_index("core") - c_a) % 2) * 32
        + ((lax.axis_index("x") - x_a) % 4) * 8
        + (lax.axis_index("zl") - zl_a) % 8
    )
    down_parts = slabs[:, cut[2] : cut[3]].reshape((64,) + pieces[2].shape)[slot]
    down_t = down_parts.reshape(64 * pieces[2].shape[0], pieces[2].shape[1])
    rows3, width3, chans3 = u3.shape
    rows2, cols2, chans2 = y2.shape
    grad_u3 = block_grad(
        u3.reshape(-1, chans3),
        g3.reshape(-1, chans3),
        ln3_w,
        ln3_b,
        bias3,
        gamma3,
        expand3,
        project3,
    ).reshape(u3.shape)
    rimmed3 = padded_2(grad_u3, ((ROW + COL, 0),), 3)
    padded3 = jnp.pad(rimmed3, ((0, 0), (3, 3), (0, 0)))
    gx3 = (g3.astype(jnp.float32) + spread(padded3, kernel3, rows3, width3)).astype(jnp.bfloat16)
    moved = lax.all_to_all(gx3, COL, split_axis=1, concat_axis=0, tiled=True)
    grad_m = project_down(moved.reshape(-1, chans3), down_t).astype(jnp.bfloat16)
    grad_mf = grad_m.astype(jnp.float32)
    grad_mf = (
        grad_mf.reshape(rows2 // 2, cols2 // 2, 2, 2, chans2)
        .transpose(0, 2, 1, 3, 4)
        .reshape(rows2, cols2, chans2)
    )
    grad_y = norm_back(y2, grad_mf, dln_w)
    tile_rows, tile_cols = tissue.shape
    pixel_mask = jnp.broadcast_to(
        tissue.astype(jnp.float32)[:, None, :, None], (tile_rows, TILE, tile_cols, TILE)
    ).reshape(rows2, cols2)
    g2 = (grad_y * pixel_mask[:, :, None]).astype(jnp.bfloat16)
    grad_u2 = block_grad(
        u2.reshape(-1, chans2),
        g2.reshape(-1, chans2),
        ln2_w,
        ln2_b,
        bias2,
        gamma2,
        expand2,
        project2,
    ).reshape(u2.shape)
    padded2 = padded_2(grad_u2, ((ROW, 0), (COL, 1)), 3)
    return (g2.astype(jnp.float32) + spread(padded2, kernel2, rows2, cols2)).astype(jnp.bfloat16)


def solution(mesh):
    sizes = tuple(n for _, n in STAGES) + (4, 2)
    mesh = Mesh(mesh.devices.reshape(sizes), ROW + COL)
    placed = (
        P(ROW + COL, None, None),
        P(ROW + COL, None, None),
        P(),
        P(),
        P(),
        P(),
        P(),
        P(None, ROW),
        P(None, ROW),
        P(None, ROW),
        P(),
        P(ROW, COL, None),
        P(ROW, COL, None),
        P(),
        P(),
        P(),
        P(),
        P(),
        P(None, ROW),
        P(None, ROW),
        P(ROW, COL),
    )
    return jax.shard_map(
        on_device, mesh=mesh, in_specs=placed, out_specs=P(ROW, COL, None), check_vma=False
    )
```

```python
import jax
import jax.numpy as jnp
from jax import lax
from jax.sharding import Mesh
from jax.sharding import PartitionSpec as P


ROW = ("zl", "x", "core")
COL = ("y", "zh")
STAGES = (("zl", 8), ("x", 4), ("core", 2))

TILE = 16


EPS = 1e-06
ROOT_HALF = 0.7071067811865476
DENS = 0.3989422804014327


def padded_2(block, sides, width):
    for axis, dim in sides:
        count = lax.axis_size(axis)
        forward = [(i, i + 1) for i in range(count - 1)]
        backward = [(target, source) for source, target in forward]
        low = lax.ppermute(
            lax.slice_in_dim(block, block.shape[dim] - width, None, axis=dim), axis, forward
        )
        high = lax.ppermute(lax.slice_in_dim(block, 0, width, axis=dim), axis, backward)
        block = jnp.concatenate([low, block, high], axis=dim)
    return block


def shifted_gather(block, axis, count):
    parts = [block]
    for shift in range(1, count):
        pairs = [(i, (i + shift) % count) for i in range(count)]
        parts.append(lax.ppermute(block, axis, pairs))
    return jnp.concatenate(parts, axis=0)


def ring_gather(block):
    def lin(z):
        return (z % 8) * 2 + z // 8

    parts = [block]
    for shift in range(1, 8):
        step = shift if shift <= 4 else shift - 8
        pairs = [(lin(z), lin((z + step) % 16)) for z in range(16)]
        parts.append(lax.ppermute(block, ("zl", "zh"), pairs))
    return jnp.concatenate(parts, axis=0)


def gather_weights(pieces):
    flat = jnp.concatenate([p.reshape(-1, 512) for p in pieces], axis=0)
    flat = ring_gather(flat)
    for axis, count in STAGES[1:]:
        flat = shifted_gather(flat, axis, count)
    slabs = flat.reshape(64, -1, 512)
    r = jnp.arange(64)
    s_core, s_x, s_zl = r // 32, (r // 8) % 4, r % 8
    zl = (lax.axis_index("zl") - s_zl) % 8
    xx = (lax.axis_index("x") - s_x) % 4
    cc = (lax.axis_index("core") - s_core) % 2
    source = (zl * 4 + xx) * 2 + cc
    return slabs, source


def block_grad(u, g, layernorm_weight, layernorm_bias, bias, gamma, expand_t, project_t):
    def one(pair):
        ub, gb = pair
        uf = ub.astype(jnp.float32)
        centered_input = uf - jnp.mean(uf, axis=-1, keepdims=True)
        inverse_deviation = lax.rsqrt(
            jnp.mean(centered_input * centered_input, axis=-1, keepdims=True) + EPS
        )
        standardized_input = centered_input * inverse_deviation
        normalized_output = (standardized_input * layernorm_weight + layernorm_bias).astype(
            jnp.bfloat16
        )
        hidden = (
            lax.dot_general(
                normalized_output, expand_t, (((1,), (1,)), ((), ())),
                preferred_element_type=jnp.float32,
            )
            + bias
        )
        scaled = (gamma * gb.astype(jnp.float32)).astype(jnp.bfloat16)
        grad_act = lax.dot_general(
            scaled, project_t, (((1,), (1,)), ((), ())), preferred_element_type=jnp.float32
        )
        slope = 0.5 * (1.0 + jax.scipy.special.erf(hidden * ROOT_HALF)) + hidden * DENS * jnp.exp(
            -0.5 * hidden * hidden
        )
        grad_hid = (grad_act * slope).astype(jnp.bfloat16)
        grad_norm = jnp.dot(grad_hid, expand_t, preferred_element_type=jnp.float32)
        projection_term = grad_norm * layernorm_weight
        upstream_gradient = inverse_deviation * (
            projection_term
            - jnp.mean(projection_term, axis=-1, keepdims=True)
            - standardized_input
            * jnp.mean(projection_term * standardized_input, axis=-1, keepdims=True)
        )
        return upstream_gradient.astype(jnp.bfloat16)

    return one((u, g))


def spread(padded, kernel, height, width):
    total = jnp.zeros((height, width, padded.shape[2]), jnp.float32)
    for dy in range(7):
        for dx in range(7):
            total = total + kernel[dy, dx] * padded[
                6 - dy : 6 - dy + height, 6 - dx : 6 - dx + width
            ].astype(jnp.float32)
    return total


def norm_back(value, grad, gain):
    vf = value.astype(jnp.float32)
    centered_input = vf - jnp.mean(vf, axis=-1, keepdims=True)
    inverse_deviation = lax.rsqrt(
        jnp.mean(centered_input * centered_input, axis=-1, keepdims=True) + EPS
    )
    yhat = centered_input * inverse_deviation
    projection_term = grad * gain
    return inverse_deviation * (
        projection_term
        - jnp.mean(projection_term, axis=-1, keepdims=True)
        - yhat * jnp.mean(projection_term * yhat, axis=-1, keepdims=True)
    )


def project_down(grads, down_t):
    return jnp.dot(grads, down_t, preferred_element_type=jnp.float32)


def on_device(
    u3,
    g3,
    ln3_w,
    ln3_b,
    bias3,
    gamma3,
    kernel3,
    expand3,
    project3,
    down_w,
    dln_w,
    y2,
    u2,
    ln2_w,
    ln2_b,
    bias2,
    gamma2,
    kernel2,
    expand2,
    project2,
    tissue,
):
    pieces = (expand3.T, project3.T, down_w.T, expand2.T, project2.T)
    slabs, source = gather_weights(pieces)
    cut = [0]
    for p in pieces:
        cut.append(cut[-1] + p.size // 512)

    def stacked(i):
        part = slabs[:, cut[i] : cut[i + 1]].reshape((64,) + pieces[i].shape)
        return part.reshape(64 * pieces[i].shape[0], pieces[i].shape[1])

    expand3 = stacked(0)
    project3 = stacked(1)
    expand2 = stacked(3)
    project2 = stacked(4)
    bias3 = bias3.reshape(64, -1)[source].reshape(-1)
    bias2 = bias2.reshape(64, -1)[source].reshape(-1)
    r = jnp.arange(64)
    zl_a, x_a, c_a = r // 8, (r // 2) % 4, r % 2
    slot = (
        ((lax.axis_index("core") - c_a) % 2) * 32
        + ((lax.axis_index("x") - x_a) % 4) * 8
        + (lax.axis_index("zl") - zl_a) % 8
    )
    down_parts = slabs[:, cut[2] : cut[3]].reshape((64,) + pieces[2].shape)[slot]
    down_t = down_parts.reshape(64 * pieces[2].shape[0], pieces[2].shape[1])
    chans3 = u3.shape[-1]
    both = jnp.concatenate([u3, g3], axis=-1)
    both = lax.all_to_all(both, COL, split_axis=1, concat_axis=0, tiled=True)
    u3, g3 = both[..., :chans3], both[..., chans3:]
    rows3, width3, chans3 = u3.shape
    rows2, cols2, chans2 = y2.shape
    grad_u3 = block_grad(
        u3.reshape(-1, chans3),
        g3.reshape(-1, chans3),
        ln3_w,
        ln3_b,
        bias3,
        gamma3,
        expand3,
        project3,
    ).reshape(u3.shape)
    padded3 = padded_2(grad_u3, ((ROW, 0), (COL, 1)), 3)
    gx3 = (g3.astype(jnp.float32) + spread(padded3, kernel3, rows3, width3)).astype(jnp.bfloat16)
    grad_m = project_down(gx3.reshape(-1, chans3), down_t).astype(jnp.bfloat16)
    grad_mf = grad_m.astype(jnp.float32)
    grad_mf = (
        grad_mf.reshape(rows2 // 2, cols2 // 2, 2, 2, chans2)
        .transpose(0, 2, 1, 3, 4)
        .reshape(rows2, cols2, chans2)
    )
    grad_y = norm_back(y2, grad_mf, dln_w)
    tile_rows, tile_cols = tissue.shape
    pixel_mask = jnp.broadcast_to(
        tissue.astype(jnp.float32)[:, None, :, None], (tile_rows, TILE, tile_cols, TILE)
    ).reshape(rows2, cols2)
    g2 = (grad_y * pixel_mask[:, :, None]).astype(jnp.bfloat16)
    grad_u2 = block_grad(
        u2.reshape(-1, chans2),
        g2.reshape(-1, chans2),
        ln2_w,
        ln2_b,
        bias2,
        gamma2,
        expand2,
        project2,
    ).reshape(u2.shape)
    padded2 = padded_2(grad_u2, ((ROW, 0), (COL, 1)), 3)
    return (g2.astype(jnp.float32) + spread(padded2, kernel2, rows2, cols2)).astype(jnp.bfloat16)


def solution(mesh):
    sizes = tuple(n for _, n in STAGES) + (4, 2)
    mesh = Mesh(mesh.devices.reshape(sizes), ROW + COL)
    placed = (
        P(ROW + COL, None, None),
        P(ROW + COL, None, None),
        P(),
        P(),
        P(),
        P(),
        P(),
        P(None, ROW),
        P(None, ROW),
        P(None, ROW),
        P(),
        P(ROW, COL, None),
        P(ROW, COL, None),
        P(),
        P(),
        P(),
        P(),
        P(),
        P(None, ROW),
        P(None, ROW),
        P(ROW, COL),
    )
    return jax.shard_map(
        on_device, mesh=mesh, in_specs=placed, out_specs=P(ROW, COL, None), check_vma=False
    )
```

```python
import jax
import jax.numpy as jnp
from jax import lax
from jax.sharding import Mesh
from jax.sharding import PartitionSpec as P


ROW = ("zl", "x", "core")
COL = ("y", "zh")
STAGES = (("zl", 8), ("x", 4), ("core", 2))

TILE = 16


EPS = 1e-06
ROOT_HALF = 0.7071067811865476
DENS = 0.3989422804014327


def padded_2(block, sides, width):
    for axis, dim in sides:
        count = lax.axis_size(axis)
        forward = [(i, i + 1) for i in range(count - 1)]
        backward = [(target, source) for source, target in forward]
        low = lax.ppermute(
            lax.slice_in_dim(block, block.shape[dim] - width, None, axis=dim), axis, forward
        )
        high = lax.ppermute(lax.slice_in_dim(block, 0, width, axis=dim), axis, backward)
        block = jnp.concatenate([low, block, high], axis=dim)
    return block


def shifted_gather(block, axis, count):
    parts = [block]
    for shift in range(1, count):
        pairs = [(i, (i + shift) % count) for i in range(count)]
        parts.append(lax.ppermute(block, axis, pairs))
    return jnp.concatenate(parts, axis=0)


def ring_gather(block):
    def lin(z):
        return (z % 8) * 2 + z // 8

    def hop(value, step):
        pairs = [(lin(z), lin((z + step) % 16)) for z in range(16)]
        return lax.ppermute(value, ("zl", "zh"), pairs)

    half = block.shape[0] // 2
    from_1, from_m1 = hop(block, 1), hop(block, -1)
    from_2, from_m2 = hop(block, 2), hop(block, -2)
    from_3, from_m3 = hop(from_1, 2), hop(from_m1, -2)
    from_4 = jnp.concatenate([hop(from_2[:half], 2), hop(from_m2[half:], -2)], axis=0)
    parts = [block, from_1, from_2, from_3, from_4, from_m3, from_m2, from_m1]
    return jnp.concatenate(parts, axis=0)


def ring_gather_4(block, axis):
    def hop(value, step):
        return lax.ppermute(value, axis, [(i, (i + step) % 4) for i in range(4)])

    half = block.shape[0] // 2
    from_1, from_m1 = hop(block, 1), hop(block, -1)
    from_2 = jnp.concatenate([hop(from_1[:half], 1), hop(from_m1[half:], -1)], axis=0)
    return jnp.concatenate([block, from_1, from_2, from_m1], axis=0)


def gather_weights(pieces):
    flat = jnp.concatenate([p.reshape(-1, 512) for p in pieces], axis=0)
    flat = ring_gather(flat)
    flat = ring_gather_4(flat, "x")
    flat = shifted_gather(flat, "core", 2)
    slabs = flat.reshape(64, -1, 512)
    r = jnp.arange(64)
    s_core, s_x, s_zl = r // 32, (r // 8) % 4, r % 8
    zl = (lax.axis_index("zl") - s_zl) % 8
    xx = (lax.axis_index("x") - s_x) % 4
    cc = (lax.axis_index("core") - s_core) % 2
    source = (zl * 4 + xx) * 2 + cc
    return slabs, source


def block_grad(u, g, layernorm_weight, layernorm_bias, bias, gamma, expand_t, project_t):
    def one(pair):
        ub, gb = pair
        uf = ub.astype(jnp.float32)
        centered_input = uf - jnp.mean(uf, axis=-1, keepdims=True)
        inverse_deviation = lax.rsqrt(
            jnp.mean(centered_input * centered_input, axis=-1, keepdims=True) + EPS
        )
        standardized_input = centered_input * inverse_deviation
        normalized_output = (standardized_input * layernorm_weight + layernorm_bias).astype(
            jnp.bfloat16
        )
        hidden = (
            lax.dot_general(
                normalized_output, expand_t, (((1,), (1,)), ((), ())),
                preferred_element_type=jnp.float32,
            )
            + bias
        )
        scaled = (gamma * gb.astype(jnp.float32)).astype(jnp.bfloat16)
        grad_act = lax.dot_general(
            scaled, project_t, (((1,), (1,)), ((), ())), preferred_element_type=jnp.float32
        )
        slope = 0.5 * (1.0 + jax.scipy.special.erf(hidden * ROOT_HALF)) + hidden * DENS * jnp.exp(
            -0.5 * hidden * hidden
        )
        grad_hid = (grad_act * slope).astype(jnp.bfloat16)
        grad_norm = jnp.dot(grad_hid, expand_t, preferred_element_type=jnp.float32)
        projection_term = grad_norm * layernorm_weight
        upstream_gradient = inverse_deviation * (
            projection_term
            - jnp.mean(projection_term, axis=-1, keepdims=True)
            - standardized_input
            * jnp.mean(projection_term * standardized_input, axis=-1, keepdims=True)
        )
        return upstream_gradient.astype(jnp.bfloat16)

    return one((u, g))


def spread(padded, kernel, height, width):
    total = jnp.zeros((height, width, padded.shape[2]), jnp.float32)
    for dy in range(7):
        for dx in range(7):
            total = total + kernel[dy, dx] * padded[
                6 - dy : 6 - dy + height, 6 - dx : 6 - dx + width
            ].astype(jnp.float32)
    return total


def norm_back(value, grad, gain):
    vf = value.astype(jnp.float32)
    centered_input = vf - jnp.mean(vf, axis=-1, keepdims=True)
    inverse_deviation = lax.rsqrt(
        jnp.mean(centered_input * centered_input, axis=-1, keepdims=True) + EPS
    )
    yhat = centered_input * inverse_deviation
    projection_term = grad * gain
    return inverse_deviation * (
        projection_term
        - jnp.mean(projection_term, axis=-1, keepdims=True)
        - yhat * jnp.mean(projection_term * yhat, axis=-1, keepdims=True)
    )


def project_down(grads, down_t):
    return jnp.dot(grads, down_t, preferred_element_type=jnp.float32)


def on_device(
    u3,
    g3,
    ln3_w,
    ln3_b,
    bias3,
    gamma3,
    kernel3,
    expand3,
    project3,
    down_w,
    dln_w,
    y2,
    u2,
    ln2_w,
    ln2_b,
    bias2,
    gamma2,
    kernel2,
    expand2,
    project2,
    tissue,
):
    pieces = (expand3.T, project3.T, down_w.T, expand2.T, project2.T)
    slabs, source = gather_weights(pieces)
    cut = [0]
    for p in pieces:
        cut.append(cut[-1] + p.size // 512)

    def stacked(i):
        part = slabs[:, cut[i] : cut[i + 1]].reshape((64,) + pieces[i].shape)
        return part.reshape(64 * pieces[i].shape[0], pieces[i].shape[1])

    expand3 = stacked(0)
    project3 = stacked(1)
    expand2 = stacked(3)
    project2 = stacked(4)
    bias3 = bias3.reshape(64, -1)[source].reshape(-1)
    bias2 = bias2.reshape(64, -1)[source].reshape(-1)
    r = jnp.arange(64)
    zl_a, x_a, c_a = r // 8, (r // 2) % 4, r % 2
    slot = (
        ((lax.axis_index("core") - c_a) % 2) * 32
        + ((lax.axis_index("x") - x_a) % 4) * 8
        + (lax.axis_index("zl") - zl_a) % 8
    )
    down_parts = slabs[:, cut[2] : cut[3]].reshape((64,) + pieces[2].shape)[slot]
    down_t = down_parts.reshape(64 * pieces[2].shape[0], pieces[2].shape[1])
    chans3 = u3.shape[-1]
    both = jnp.concatenate([u3, g3], axis=-1)
    both = lax.all_to_all(both, COL, split_axis=1, concat_axis=0, tiled=True)
    u3, g3 = both[..., :chans3], both[..., chans3:]
    rows3, width3, chans3 = u3.shape
    rows2, cols2, chans2 = y2.shape
    grad_u3 = block_grad(
        u3.reshape(-1, chans3),
        g3.reshape(-1, chans3),
        ln3_w,
        ln3_b,
        bias3,
        gamma3,
        expand3,
        project3,
    ).reshape(u3.shape)
    padded3 = padded_2(grad_u3, ((ROW, 0), (COL, 1)), 3)
    gx3 = (g3.astype(jnp.float32) + spread(padded3, kernel3, rows3, width3)).astype(jnp.bfloat16)
    grad_m = project_down(gx3.reshape(-1, chans3), down_t).astype(jnp.bfloat16)
    grad_mf = grad_m.astype(jnp.float32)
    grad_mf = (
        grad_mf.reshape(rows2 // 2, cols2 // 2, 2, 2, chans2)
        .transpose(0, 2, 1, 3, 4)
        .reshape(rows2, cols2, chans2)
    )
    grad_y = norm_back(y2, grad_mf, dln_w)
    tile_rows, tile_cols = tissue.shape
    pixel_mask = jnp.broadcast_to(
        tissue.astype(jnp.float32)[:, None, :, None], (tile_rows, TILE, tile_cols, TILE)
    ).reshape(rows2, cols2)
    g2 = (grad_y * pixel_mask[:, :, None]).astype(jnp.bfloat16)
    grad_u2 = block_grad(
        u2.reshape(-1, chans2),
        g2.reshape(-1, chans2),
        ln2_w,
        ln2_b,
        bias2,
        gamma2,
        expand2,
        project2,
    ).reshape(u2.shape)
    padded2 = padded_2(grad_u2, ((ROW, 0), (COL, 1)), 3)
    return (g2.astype(jnp.float32) + spread(padded2, kernel2, rows2, cols2)).astype(jnp.bfloat16)


def solution(mesh):
    sizes = tuple(n for _, n in STAGES) + (4, 2)
    mesh = Mesh(mesh.devices.reshape(sizes), ROW + COL)
    placed = (
        P(ROW + COL, None, None),
        P(ROW + COL, None, None),
        P(),
        P(),
        P(),
        P(),
        P(),
        P(None, ROW),
        P(None, ROW),
        P(None, ROW),
        P(),
        P(ROW, COL, None),
        P(ROW, COL, None),
        P(),
        P(),
        P(),
        P(),
        P(),
        P(None, ROW),
        P(None, ROW),
        P(ROW, COL),
    )
    return jax.shard_map(
        on_device, mesh=mesh, in_specs=placed, out_specs=P(ROW, COL, None), check_vma=False
    )
```

```python
import jax
import jax.numpy as jnp
from jax import lax
from jax.sharding import Mesh
from jax.sharding import PartitionSpec as P


ROW = ("zl", "x", "core")
COL = ("y", "zh")
STAGES = (("zl", 8), ("x", 4), ("core", 2))

TILE = 16


EPS = 1e-06
ROOT_HALF = 0.7071067811865476
DENS = 0.3989422804014327


def padded_2(block, sides, width):
    for axis, dim in sides:
        count = lax.axis_size(axis)
        forward = [(i, i + 1) for i in range(count - 1)]
        backward = [(target, source) for source, target in forward]
        low = lax.ppermute(
            lax.slice_in_dim(block, block.shape[dim] - width, None, axis=dim), axis, forward
        )
        high = lax.ppermute(lax.slice_in_dim(block, 0, width, axis=dim), axis, backward)
        block = jnp.concatenate([low, block, high], axis=dim)
    return block


def shifted_gather(block, axis, count):
    parts = [block]
    for shift in range(1, count):
        pairs = [(i, (i + shift) % count) for i in range(count)]
        parts.append(lax.ppermute(block, axis, pairs))
    return jnp.concatenate(parts, axis=0)


def ring_gather(block):
    def lin(z):
        return (z % 8) * 2 + z // 8

    def hop(value, step):
        pairs = [(lin(z), lin((z + step) % 16)) for z in range(16)]
        return lax.ppermute(value, ("zl", "zh"), pairs)

    half = block.shape[0] // 2
    from_1, from_m1 = hop(block, 1), hop(block, -1)
    from_2, from_m2 = hop(block, 2), hop(block, -2)
    from_3, from_m3 = hop(from_1, 2), hop(from_m1, -2)
    from_4 = jnp.concatenate([hop(from_2[:half], 2), hop(from_m2[half:], -2)], axis=0)
    parts = [block, from_1, from_2, from_3, from_4, from_m3, from_m2, from_m1]
    return jnp.concatenate(parts, axis=0)


def ring_gather_4(block, axis):
    def hop(value, step):
        return lax.ppermute(value, axis, [(i, (i + step) % 4) for i in range(4)])

    half = block.shape[0] // 2
    from_1, from_m1 = hop(block, 1), hop(block, -1)
    from_2 = jnp.concatenate([hop(from_1[:half], 1), hop(from_m1[half:], -1)], axis=0)
    return jnp.concatenate([block, from_1, from_2, from_m1], axis=0)


def gather_weights(pieces):
    flat = jnp.concatenate([p.reshape(-1, 512) for p in pieces], axis=0)
    flat = ring_gather(flat)
    flat = ring_gather_4(flat, "x")
    flat = shifted_gather(flat, "core", 2)
    slabs = flat.reshape(64, -1, 512)
    r = jnp.arange(64)
    s_core, s_x, s_zl = r // 32, (r // 8) % 4, r % 8
    zl = (lax.axis_index("zl") - s_zl) % 8
    xx = (lax.axis_index("x") - s_x) % 4
    cc = (lax.axis_index("core") - s_core) % 2
    source = (zl * 4 + xx) * 2 + cc
    return slabs, source


def block_grad(u, g, layernorm_weight, layernorm_bias, bias, gamma, expand_t, project_t):
    def one(pair):
        ub, gb = pair
        uf = ub.astype(jnp.float32)
        centered_input = uf - jnp.mean(uf, axis=-1, keepdims=True)
        inverse_deviation = lax.rsqrt(
            jnp.mean(centered_input * centered_input, axis=-1, keepdims=True) + EPS
        )
        standardized_input = centered_input * inverse_deviation
        normalized_output = (standardized_input * layernorm_weight + layernorm_bias).astype(
            jnp.bfloat16
        )
        hidden = (
            lax.dot_general(
                normalized_output, expand_t, (((1,), (1,)), ((), ())),
                preferred_element_type=jnp.float32,
            )
            + bias
        )
        scaled = (gamma * gb.astype(jnp.float32)).astype(jnp.bfloat16)
        grad_act = lax.dot_general(
            scaled, project_t, (((1,), (1,)), ((), ())), preferred_element_type=jnp.float32
        )
        slope = 0.5 * (1.0 + jax.scipy.special.erf(hidden * ROOT_HALF)) + hidden * DENS * jnp.exp(
            -0.5 * hidden * hidden
        )
        grad_hid = (grad_act * slope).astype(jnp.bfloat16)
        grad_norm = jnp.dot(grad_hid, expand_t, preferred_element_type=jnp.float32)
        projection_term = grad_norm * layernorm_weight
        upstream_gradient = inverse_deviation * (
            projection_term
            - jnp.mean(projection_term, axis=-1, keepdims=True)
            - standardized_input
            * jnp.mean(projection_term * standardized_input, axis=-1, keepdims=True)
        )
        return upstream_gradient.astype(jnp.bfloat16)

    return one((u, g))


def spread(padded, kernel, height, width):
    total = jnp.zeros((height, width, padded.shape[2]), jnp.float32)
    for dy in range(7):
        for dx in range(7):
            total = total + kernel[dy, dx] * padded[
                6 - dy : 6 - dy + height, 6 - dx : 6 - dx + width
            ].astype(jnp.float32)
    return total


def norm_back(value, grad, gain):
    vf = value.astype(jnp.float32)
    centered_input = vf - jnp.mean(vf, axis=-1, keepdims=True)
    inverse_deviation = lax.rsqrt(
        jnp.mean(centered_input * centered_input, axis=-1, keepdims=True) + EPS
    )
    yhat = centered_input * inverse_deviation
    projection_term = grad * gain
    return inverse_deviation * (
        projection_term
        - jnp.mean(projection_term, axis=-1, keepdims=True)
        - yhat * jnp.mean(projection_term * yhat, axis=-1, keepdims=True)
    )


def project_down(grads, down_t):
    return jnp.dot(grads, down_t, preferred_element_type=jnp.float32)


def on_device(
    u3,
    g3,
    ln3_w,
    ln3_b,
    bias3,
    gamma3,
    kernel3,
    expand3,
    project3,
    down_w,
    dln_w,
    y2,
    u2,
    ln2_w,
    ln2_b,
    bias2,
    gamma2,
    kernel2,
    expand2,
    project2,
    tissue,
):
    pieces = (expand3.T, project3.T, down_w.T, expand2.T, project2.T)
    slabs, source = gather_weights(pieces)
    cut = [0]
    for p in pieces:
        cut.append(cut[-1] + p.size // 512)

    def stacked(i):
        part = slabs[:, cut[i] : cut[i + 1]].reshape((64,) + pieces[i].shape)
        return part.reshape(64 * pieces[i].shape[0], pieces[i].shape[1])

    expand3 = stacked(0)
    project3 = stacked(1)
    expand2 = stacked(3)
    project2 = stacked(4)
    bias3 = bias3.reshape(64, -1)[source].reshape(-1)
    bias2 = bias2.reshape(64, -1)[source].reshape(-1)
    r = jnp.arange(64)
    zl_a, x_a, c_a = r // 8, (r // 2) % 4, r % 2
    slot = (
        ((lax.axis_index("core") - c_a) % 2) * 32
        + ((lax.axis_index("x") - x_a) % 4) * 8
        + (lax.axis_index("zl") - zl_a) % 8
    )
    down_parts = slabs[:, cut[2] : cut[3]].reshape((64,) + pieces[2].shape)[slot]
    down_t = down_parts.reshape(64 * pieces[2].shape[0], pieces[2].shape[1])
    chans3 = u3.shape[-1]
    both = jnp.concatenate([u3, g3], axis=-1)
    both = lax.all_to_all(both, COL, split_axis=1, concat_axis=0, tiled=True)
    u3, g3 = both[..., :chans3], both[..., chans3:]
    rows3, width3, chans3 = u3.shape
    rows2, cols2, chans2 = y2.shape
    grad_u3 = block_grad(
        u3.reshape(-1, chans3),
        g3.reshape(-1, chans3),
        ln3_w,
        ln3_b,
        bias3,
        gamma3,
        expand3,
        project3,
    ).reshape(u3.shape)
    padded3 = padded_2(grad_u3, ((ROW, 0), (COL, 1)), 3)
    gx3 = (g3.astype(jnp.float32) + spread(padded3, kernel3, rows3, width3)).astype(jnp.bfloat16)
    grad_m = project_down(gx3.reshape(-1, chans3), down_t).astype(jnp.bfloat16)
    grad_mf = grad_m.astype(jnp.float32)
    grad_mf = (
        grad_mf.reshape(rows2 // 2, cols2 // 2, 2, 2, chans2)
        .transpose(0, 2, 1, 3, 4)
        .reshape(rows2, cols2, chans2)
    )
    grad_y = norm_back(y2, grad_mf, dln_w)
    tile_rows, tile_cols = tissue.shape
    pixel_mask = jnp.broadcast_to(
        tissue.astype(jnp.float32)[:, None, :, None], (tile_rows, TILE, tile_cols, TILE)
    ).reshape(rows2, cols2)
    g2 = (grad_y * pixel_mask[:, :, None]).astype(jnp.bfloat16)
    grad_u2 = block_grad(
        u2.reshape(-1, chans2),
        g2.reshape(-1, chans2),
        ln2_w,
        ln2_b,
        bias2,
        gamma2,
        expand2,
        project2,
    ).reshape(u2.shape)
    rimmed2 = padded_2(grad_u2, ((ROW, 0),), 3)
    padded2 = padded_2(rimmed2, ((COL, 1),), 3)
    inner = spread(rimmed2, kernel2, rows2, cols2 - 6)
    left = spread(padded2[:, :9], kernel2, rows2, 3)
    right = spread(padded2[:, cols2 - 3 :], kernel2, rows2, 3)
    total = jnp.concatenate([left, inner, right], axis=1)
    return (g2.astype(jnp.float32) + total).astype(jnp.bfloat16)


def solution(mesh):
    sizes = tuple(n for _, n in STAGES) + (4, 2)
    mesh = Mesh(mesh.devices.reshape(sizes), ROW + COL)
    placed = (
        P(ROW + COL, None, None),
        P(ROW + COL, None, None),
        P(),
        P(),
        P(),
        P(),
        P(),
        P(None, ROW),
        P(None, ROW),
        P(None, ROW),
        P(),
        P(ROW, COL, None),
        P(ROW, COL, None),
        P(),
        P(),
        P(),
        P(),
        P(),
        P(None, ROW),
        P(None, ROW),
        P(ROW, COL),
    )
    return jax.shard_map(
        on_device, mesh=mesh, in_specs=placed, out_specs=P(ROW, COL, None), check_vma=False
    )
```

```python
import jax
import jax.numpy as jnp
from jax import lax
from jax.sharding import Mesh
from jax.sharding import PartitionSpec as P


ROW = ("zl", "x", "core")
COL = ("y", "zh")
STAGES = (("zl", 8), ("x", 4), ("core", 2))

TILE = 16


EPS = 1e-06
ROOT_HALF = 0.7071067811865476
DENS = 0.3989422804014327


def padded_2(block, sides, width):
    for axis, dim in sides:
        count = lax.axis_size(axis)
        forward = [(i, i + 1) for i in range(count - 1)]
        backward = [(target, source) for source, target in forward]
        low = lax.ppermute(
            lax.slice_in_dim(block, block.shape[dim] - width, None, axis=dim), axis, forward
        )
        high = lax.ppermute(lax.slice_in_dim(block, 0, width, axis=dim), axis, backward)
        block = jnp.concatenate([low, block, high], axis=dim)
    return block


def shifted_gather(block, axis, count):
    parts = [block]
    for shift in range(1, count):
        pairs = [(i, (i + shift) % count) for i in range(count)]
        parts.append(lax.ppermute(block, axis, pairs))
    return jnp.concatenate(parts, axis=0)


def ring_gather(block):
    def lin(z):
        return (z % 8) * 2 + z // 8

    def hop(value, step):
        pairs = [(lin(z), lin((z + step) % 16)) for z in range(16)]
        return lax.ppermute(value, ("zl", "zh"), pairs)

    half = block.shape[0] // 2
    from_1, from_m1 = hop(block, 1), hop(block, -1)
    from_2, from_m2 = hop(from_1, 1), hop(from_m1, -1)
    from_3, from_m3 = hop(from_2, 1), hop(from_m2, -1)
    from_4 = jnp.concatenate([hop(from_3[:half], 1), hop(from_m3[half:], -1)], axis=0)
    parts = [block, from_1, from_2, from_3, from_4, from_m3, from_m2, from_m1]
    return jnp.concatenate(parts, axis=0)


def ring_gather_4(block, axis):
    def hop(value, step):
        return lax.ppermute(value, axis, [(i, (i + step) % 4) for i in range(4)])

    half = block.shape[0] // 2
    from_1, from_m1 = hop(block, 1), hop(block, -1)
    from_2 = jnp.concatenate([hop(from_1[:half], 1), hop(from_m1[half:], -1)], axis=0)
    return jnp.concatenate([block, from_1, from_2, from_m1], axis=0)


def gather_weights(pieces):
    flat = jnp.concatenate([p.reshape(-1, 512) for p in pieces], axis=0)
    flat = ring_gather(flat)
    flat = ring_gather_4(flat, "x")
    flat = shifted_gather(flat, "core", 2)
    slabs = flat.reshape(64, -1, 512)
    r = jnp.arange(64)
    s_core, s_x, s_zl = r // 32, (r // 8) % 4, r % 8
    zl = (lax.axis_index("zl") - s_zl) % 8
    xx = (lax.axis_index("x") - s_x) % 4
    cc = (lax.axis_index("core") - s_core) % 2
    source = (zl * 4 + xx) * 2 + cc
    return slabs, source


def block_grad(u, g, layernorm_weight, layernorm_bias, bias, gamma, expand_t, project_t):
    def one(pair):
        ub, gb = pair
        uf = ub.astype(jnp.float32)
        centered_input = uf - jnp.mean(uf, axis=-1, keepdims=True)
        inverse_deviation = lax.rsqrt(
            jnp.mean(centered_input * centered_input, axis=-1, keepdims=True) + EPS
        )
        standardized_input = centered_input * inverse_deviation
        normalized_output = (standardized_input * layernorm_weight + layernorm_bias).astype(
            jnp.bfloat16
        )
        hidden = (
            lax.dot_general(
                normalized_output, expand_t, (((1,), (1,)), ((), ())),
                preferred_element_type=jnp.float32,
            )
            + bias
        )
        scaled = (gamma * gb.astype(jnp.float32)).astype(jnp.bfloat16)
        grad_act = lax.dot_general(
            scaled, project_t, (((1,), (1,)), ((), ())), preferred_element_type=jnp.float32
        )
        slope = 0.5 * (1.0 + jax.scipy.special.erf(hidden * ROOT_HALF)) + hidden * DENS * jnp.exp(
            -0.5 * hidden * hidden
        )
        grad_hid = (grad_act * slope).astype(jnp.bfloat16)
        grad_norm = jnp.dot(grad_hid, expand_t, preferred_element_type=jnp.float32)
        projection_term = grad_norm * layernorm_weight
        upstream_gradient = inverse_deviation * (
            projection_term
            - jnp.mean(projection_term, axis=-1, keepdims=True)
            - standardized_input
            * jnp.mean(projection_term * standardized_input, axis=-1, keepdims=True)
        )
        return upstream_gradient.astype(jnp.bfloat16)

    return one((u, g))


def spread(padded, kernel, height, width):
    total = jnp.zeros((height, width, padded.shape[2]), jnp.float32)
    for dy in range(7):
        for dx in range(7):
            total = total + kernel[dy, dx] * padded[
                6 - dy : 6 - dy + height, 6 - dx : 6 - dx + width
            ].astype(jnp.float32)
    return total


def norm_back(value, grad, gain):
    vf = value.astype(jnp.float32)
    centered_input = vf - jnp.mean(vf, axis=-1, keepdims=True)
    inverse_deviation = lax.rsqrt(
        jnp.mean(centered_input * centered_input, axis=-1, keepdims=True) + EPS
    )
    yhat = centered_input * inverse_deviation
    projection_term = grad * gain
    return inverse_deviation * (
        projection_term
        - jnp.mean(projection_term, axis=-1, keepdims=True)
        - yhat * jnp.mean(projection_term * yhat, axis=-1, keepdims=True)
    )


def project_down(grads, down_t):
    return jnp.dot(grads, down_t, preferred_element_type=jnp.float32)


def on_device(
    u3,
    g3,
    ln3_w,
    ln3_b,
    bias3,
    gamma3,
    kernel3,
    expand3,
    project3,
    down_w,
    dln_w,
    y2,
    u2,
    ln2_w,
    ln2_b,
    bias2,
    gamma2,
    kernel2,
    expand2,
    project2,
    tissue,
):
    pieces = (expand3.T, project3.T, down_w.T, expand2.T, project2.T)
    slabs, source = gather_weights(pieces)
    cut = [0]
    for p in pieces:
        cut.append(cut[-1] + p.size // 512)

    def stacked(i):
        part = slabs[:, cut[i] : cut[i + 1]].reshape((64,) + pieces[i].shape)
        return part.reshape(64 * pieces[i].shape[0], pieces[i].shape[1])

    expand3 = stacked(0)
    project3 = stacked(1)
    expand2 = stacked(3)
    project2 = stacked(4)
    bias3 = bias3.reshape(64, -1)[source].reshape(-1)
    bias2 = bias2.reshape(64, -1)[source].reshape(-1)
    r = jnp.arange(64)
    zl_a, x_a, c_a = r // 8, (r // 2) % 4, r % 2
    slot = (
        ((lax.axis_index("core") - c_a) % 2) * 32
        + ((lax.axis_index("x") - x_a) % 4) * 8
        + (lax.axis_index("zl") - zl_a) % 8
    )
    down_parts = slabs[:, cut[2] : cut[3]].reshape((64,) + pieces[2].shape)[slot]
    down_t = down_parts.reshape(64 * pieces[2].shape[0], pieces[2].shape[1])
    chans3 = u3.shape[-1]
    both = jnp.concatenate([u3, g3], axis=-1)
    both = lax.all_to_all(both, COL, split_axis=1, concat_axis=0, tiled=True)
    u3, g3 = both[..., :chans3], both[..., chans3:]
    rows3, width3, chans3 = u3.shape
    rows2, cols2, chans2 = y2.shape
    grad_u3 = block_grad(
        u3.reshape(-1, chans3),
        g3.reshape(-1, chans3),
        ln3_w,
        ln3_b,
        bias3,
        gamma3,
        expand3,
        project3,
    ).reshape(u3.shape)
    padded3 = padded_2(grad_u3, ((ROW, 0), (COL, 1)), 3)
    gx3 = (g3.astype(jnp.float32) + spread(padded3, kernel3, rows3, width3)).astype(jnp.bfloat16)
    grad_m = project_down(gx3.reshape(-1, chans3), down_t).astype(jnp.bfloat16)
    grad_mf = grad_m.astype(jnp.float32)
    grad_mf = (
        grad_mf.reshape(rows2 // 2, cols2 // 2, 2, 2, chans2)
        .transpose(0, 2, 1, 3, 4)
        .reshape(rows2, cols2, chans2)
    )
    grad_y = norm_back(y2, grad_mf, dln_w)
    tile_rows, tile_cols = tissue.shape
    pixel_mask = jnp.broadcast_to(
        tissue.astype(jnp.float32)[:, None, :, None], (tile_rows, TILE, tile_cols, TILE)
    ).reshape(rows2, cols2)
    g2 = (grad_y * pixel_mask[:, :, None]).astype(jnp.bfloat16)
    grad_u2 = block_grad(
        u2.reshape(-1, chans2),
        g2.reshape(-1, chans2),
        ln2_w,
        ln2_b,
        bias2,
        gamma2,
        expand2,
        project2,
    ).reshape(u2.shape)
    padded2 = padded_2(grad_u2, ((ROW, 0), (COL, 1)), 3)
    return (g2.astype(jnp.float32) + spread(padded2, kernel2, rows2, cols2)).astype(jnp.bfloat16)


def solution(mesh):
    sizes = tuple(n for _, n in STAGES) + (4, 2)
    mesh = Mesh(mesh.devices.reshape(sizes), ROW + COL)
    placed = (
        P(ROW + COL, None, None),
        P(ROW + COL, None, None),
        P(),
        P(),
        P(),
        P(),
        P(),
        P(None, ROW),
        P(None, ROW),
        P(None, ROW),
        P(),
        P(ROW, COL, None),
        P(ROW, COL, None),
        P(),
        P(),
        P(),
        P(),
        P(),
        P(None, ROW),
        P(None, ROW),
        P(ROW, COL),
    )
    return jax.shard_map(
        on_device, mesh=mesh, in_specs=placed, out_specs=P(ROW, COL, None), check_vma=False
    )
```

```python
import jax
import jax.numpy as jnp
from jax import lax
from jax.sharding import Mesh
from jax.sharding import PartitionSpec as P


ROW = ("zl", "x", "core")
COL = ("y", "zh")
STAGES = (("zl", 8), ("x", 4), ("core", 2))

TILE = 16


EPS = 1e-06
ROOT_HALF = 0.7071067811865476
DENS = 0.3989422804014327


def padded_2(block, sides, width):
    for axis, dim in sides:
        count = lax.axis_size(axis)
        forward = [(i, i + 1) for i in range(count - 1)]
        backward = [(target, source) for source, target in forward]
        low = lax.ppermute(
            lax.slice_in_dim(block, block.shape[dim] - width, None, axis=dim), axis, forward
        )
        high = lax.ppermute(lax.slice_in_dim(block, 0, width, axis=dim), axis, backward)
        block = jnp.concatenate([low, block, high], axis=dim)
    return block


def shifted_gather(block, axis, count):
    parts = [block]
    for shift in range(1, count):
        pairs = [(i, (i + shift) % count) for i in range(count)]
        parts.append(lax.ppermute(block, axis, pairs))
    return jnp.concatenate(parts, axis=0)


def ring_gather(block):
    def lin(z):
        return (z % 8) * 2 + z // 8

    def hop(value, step):
        pairs = [(lin(z), lin((z + step) % 16)) for z in range(16)]
        return lax.ppermute(value, ("zl", "zh"), pairs)

    half = block.shape[0] // 2
    from_1, from_m1 = hop(block, 1), hop(block, -1)
    from_2, from_m2 = hop(from_1, 1), hop(from_m1, -1)
    from_3, from_m3 = hop(from_2, 1), hop(from_m2, -1)
    from_4 = jnp.concatenate([hop(from_3[:half], 1), hop(from_m3[half:], -1)], axis=0)
    parts = [block, from_1, from_2, from_3, from_4, from_m3, from_m2, from_m1]
    return jnp.concatenate(parts, axis=0)


def ring_gather_4(block, axis):
    def hop(value, step):
        return lax.ppermute(value, axis, [(i, (i + step) % 4) for i in range(4)])

    half = block.shape[0] // 2
    from_1, from_m1 = hop(block, 1), hop(block, -1)
    from_2 = jnp.concatenate([hop(from_1[:half], 1), hop(from_m1[half:], -1)], axis=0)
    return jnp.concatenate([block, from_1, from_2, from_m1], axis=0)


def gather_weights(pieces, rider):
    flat = jnp.concatenate([p.reshape(-1, 512) for p in pieces], axis=0)
    flat = ring_gather(flat)
    flat = ring_gather_4(flat, "x")
    flat, rider = lax.optimization_barrier((flat, rider))
    flat = shifted_gather(flat, "core", 2)
    slabs = flat.reshape(64, -1, 512)
    r = jnp.arange(64)
    s_core, s_x, s_zl = r // 32, (r // 8) % 4, r % 8
    zl = (lax.axis_index("zl") - s_zl) % 8
    xx = (lax.axis_index("x") - s_x) % 4
    cc = (lax.axis_index("core") - s_core) % 2
    source = (zl * 4 + xx) * 2 + cc
    return slabs, source, rider


def block_grad(u, g, layernorm_weight, layernorm_bias, bias, gamma, expand_t, project_t):
    def one(pair):
        ub, gb = pair
        uf = ub.astype(jnp.float32)
        centered_input = uf - jnp.mean(uf, axis=-1, keepdims=True)
        inverse_deviation = lax.rsqrt(
            jnp.mean(centered_input * centered_input, axis=-1, keepdims=True) + EPS
        )
        standardized_input = centered_input * inverse_deviation
        normalized_output = (standardized_input * layernorm_weight + layernorm_bias).astype(
            jnp.bfloat16
        )
        hidden = (
            lax.dot_general(
                normalized_output, expand_t, (((1,), (1,)), ((), ())),
                preferred_element_type=jnp.float32,
            )
            + bias
        )
        scaled = (gamma * gb.astype(jnp.float32)).astype(jnp.bfloat16)
        grad_act = lax.dot_general(
            scaled, project_t, (((1,), (1,)), ((), ())), preferred_element_type=jnp.float32
        )
        slope = 0.5 * (1.0 + jax.scipy.special.erf(hidden * ROOT_HALF)) + hidden * DENS * jnp.exp(
            -0.5 * hidden * hidden
        )
        grad_hid = (grad_act * slope).astype(jnp.bfloat16)
        grad_norm = jnp.dot(grad_hid, expand_t, preferred_element_type=jnp.float32)
        projection_term = grad_norm * layernorm_weight
        upstream_gradient = inverse_deviation * (
            projection_term
            - jnp.mean(projection_term, axis=-1, keepdims=True)
            - standardized_input
            * jnp.mean(projection_term * standardized_input, axis=-1, keepdims=True)
        )
        return upstream_gradient.astype(jnp.bfloat16)

    return one((u, g))


def spread(padded, kernel, height, width):
    total = jnp.zeros((height, width, padded.shape[2]), jnp.float32)
    for dy in range(7):
        for dx in range(7):
            total = total + kernel[dy, dx] * padded[
                6 - dy : 6 - dy + height, 6 - dx : 6 - dx + width
            ].astype(jnp.float32)
    return total


def norm_back(value, grad, gain):
    vf = value.astype(jnp.float32)
    centered_input = vf - jnp.mean(vf, axis=-1, keepdims=True)
    inverse_deviation = lax.rsqrt(
        jnp.mean(centered_input * centered_input, axis=-1, keepdims=True) + EPS
    )
    yhat = centered_input * inverse_deviation
    projection_term = grad * gain
    return inverse_deviation * (
        projection_term
        - jnp.mean(projection_term, axis=-1, keepdims=True)
        - yhat * jnp.mean(projection_term * yhat, axis=-1, keepdims=True)
    )


def project_down(grads, down_t):
    return jnp.dot(grads, down_t, preferred_element_type=jnp.float32)


def on_device(
    u3,
    g3,
    ln3_w,
    ln3_b,
    bias3,
    gamma3,
    kernel3,
    expand3,
    project3,
    down_w,
    dln_w,
    y2,
    u2,
    ln2_w,
    ln2_b,
    bias2,
    gamma2,
    kernel2,
    expand2,
    project2,
    tissue,
):
    pieces = (expand3.T, project3.T, down_w.T, expand2.T, project2.T)
    both = jnp.concatenate([u3, g3], axis=-1)
    slabs, source, both = gather_weights(pieces, both)
    cut = [0]
    for p in pieces:
        cut.append(cut[-1] + p.size // 512)

    def stacked(i):
        part = slabs[:, cut[i] : cut[i + 1]].reshape((64,) + pieces[i].shape)
        return part.reshape(64 * pieces[i].shape[0], pieces[i].shape[1])

    expand3 = stacked(0)
    project3 = stacked(1)
    expand2 = stacked(3)
    project2 = stacked(4)
    bias3 = bias3.reshape(64, -1)[source].reshape(-1)
    bias2 = bias2.reshape(64, -1)[source].reshape(-1)
    r = jnp.arange(64)
    zl_a, x_a, c_a = r // 8, (r // 2) % 4, r % 2
    slot = (
        ((lax.axis_index("core") - c_a) % 2) * 32
        + ((lax.axis_index("x") - x_a) % 4) * 8
        + (lax.axis_index("zl") - zl_a) % 8
    )
    down_parts = slabs[:, cut[2] : cut[3]].reshape((64,) + pieces[2].shape)[slot]
    down_t = down_parts.reshape(64 * pieces[2].shape[0], pieces[2].shape[1])
    chans3 = u3.shape[-1]
    both = lax.all_to_all(both, COL, split_axis=1, concat_axis=0, tiled=True)
    u3, g3 = both[..., :chans3], both[..., chans3:]
    rows3, width3, chans3 = u3.shape
    rows2, cols2, chans2 = y2.shape
    grad_u3 = block_grad(
        u3.reshape(-1, chans3),
        g3.reshape(-1, chans3),
        ln3_w,
        ln3_b,
        bias3,
        gamma3,
        expand3,
        project3,
    ).reshape(u3.shape)
    padded3 = padded_2(grad_u3, ((ROW, 0), (COL, 1)), 3)
    gx3 = (g3.astype(jnp.float32) + spread(padded3, kernel3, rows3, width3)).astype(jnp.bfloat16)
    grad_m = project_down(gx3.reshape(-1, chans3), down_t).astype(jnp.bfloat16)
    grad_mf = grad_m.astype(jnp.float32)
    grad_mf = (
        grad_mf.reshape(rows2 // 2, cols2 // 2, 2, 2, chans2)
        .transpose(0, 2, 1, 3, 4)
        .reshape(rows2, cols2, chans2)
    )
    grad_y = norm_back(y2, grad_mf, dln_w)
    tile_rows, tile_cols = tissue.shape
    pixel_mask = jnp.broadcast_to(
        tissue.astype(jnp.float32)[:, None, :, None], (tile_rows, TILE, tile_cols, TILE)
    ).reshape(rows2, cols2)
    g2 = (grad_y * pixel_mask[:, :, None]).astype(jnp.bfloat16)
    grad_u2 = block_grad(
        u2.reshape(-1, chans2),
        g2.reshape(-1, chans2),
        ln2_w,
        ln2_b,
        bias2,
        gamma2,
        expand2,
        project2,
    ).reshape(u2.shape)
    padded2 = padded_2(grad_u2, ((ROW, 0), (COL, 1)), 3)
    return (g2.astype(jnp.float32) + spread(padded2, kernel2, rows2, cols2)).astype(jnp.bfloat16)


def solution(mesh):
    sizes = tuple(n for _, n in STAGES) + (4, 2)
    mesh = Mesh(mesh.devices.reshape(sizes), ROW + COL)
    placed = (
        P(ROW + COL, None, None),
        P(ROW + COL, None, None),
        P(),
        P(),
        P(),
        P(),
        P(),
        P(None, ROW),
        P(None, ROW),
        P(None, ROW),
        P(),
        P(ROW, COL, None),
        P(ROW, COL, None),
        P(),
        P(),
        P(),
        P(),
        P(),
        P(None, ROW),
        P(None, ROW),
        P(ROW, COL),
    )
    return jax.shard_map(
        on_device, mesh=mesh, in_specs=placed, out_specs=P(ROW, COL, None), check_vma=False
    )
```
